32 devices in a mesh: rec: 2 (over y), gx: 16 (over z, x, core).
Axes of the slice: x: 2, y: 2, z: 4, core: 2. Of those that a mesh axis runs over, the one named last changes fastest.
Arguments:
- velocity: float32 [4, 3, 96, 16, 128], P(None, None, ('rec', 'gx')), parts along dimension 2, may hold values from -6 to 36, as said below
- span_rim: float32 [4, 2, 96, 10, 6], P(None, None, ('rec', 'gx')), parts along dimension 2, may hold values from -6 to 36, as said below
- sketch_old: bfloat16 [3, 96, 10, 128, 256], P(None, ('rec', 'gx')), parts along dimension 1, as said below
- omega: float32 [4, 256], replicated, may hold values from -6 to 6
Outputs:
- basis: bfloat16 [3, 96, 10, 128, 256], P(None, ('rec', 'gx')), parts along dimension 1
- factor: float32 [512, 256], P('rec'), parts along dimension 0
The draws below stay inside these ranges and needn't reach their ends.
There are 2 independent parts, one for each index of `rec`. The reference program is written for one: setup_inputs(seed, part) draws one part's arguments, and reference() takes and returns one part's arrays. A program takes and returns all parts, laid end to end along the dimension named above; an argument that names none is the same for every part. Nothing has to cross between parts.
Inputs may be any that keep to these rules, and one draw needn't show every extreme that they name: `sketch_old`: finite values of order one; rows differ in scale. `velocity`: finite values. `span_rim`: finite values.
All inputs are finite; a program needn't handle non-finite values.
Results may differ from the reference program's by a relative error of at most 0.014.
The reference program's roundings to bfloat16 on the way (of `sketch` and `inverse_one`) count: a program that leaves them out, or rounds other values in their place, can miss the bound.
Values sent between devices are 32-bit elements; how exact they have to be, the bound alone decides.
No kernel may reach another device: no remote copies, remote signals or barrier semaphores. Data moves between devices by JAX's collectives and lax.ppermute only.
A program may use at most 64 MiB of HBM per device.

```python
import jax
import jax.numpy as jnp
from jax import lax

RANK = 256
SNAPS = 4
NY = 10
NZ = 128
NX = 48


def flow_profile(rows, offset, base, spread):
    position = (jnp.arange(rows, dtype=jnp.float32) + offset + 0.5) / (NY + 6)
    return base + spread * jnp.tanh(2.0 * position - 1.0)


def draw_velocity(key, part):
    key_a = jax.random.fold_in(key, 21)
    shape = (SNAPS, 3, NX, NY + 6, NZ)
    values = jnp.clip(jax.random.normal(key_a, shape, jnp.float32), -6.0, 6.0)
    profile = flow_profile(NY + 6, 0, 16.0, 6.0)
    first = (jnp.arange(3, dtype=jnp.int32) == 0).astype(jnp.float32).reshape(1, 3, 1, 1, 1)
    values = values + first * profile.reshape(1, 1, 1, NY + 6, 1)
    return values.astype(jnp.float32)


def draw_span_rim(key, part):
    key_a = jax.random.fold_in(key, 31)
    shape = (SNAPS, 2, NX, NY, 6)
    values = jnp.clip(jax.random.normal(key_a, shape, jnp.float32), -6.0, 6.0)
    profile = flow_profile(NY, 3, 16.0, 6.0)
    first = (jnp.arange(2, dtype=jnp.int32) == 0).astype(jnp.float32).reshape(1, 2, 1, 1, 1)
    values = values + first * profile.reshape(1, 1, 1, NY, 1)
    return values.astype(jnp.float32)


def draw_sketch_old(key, part):
    key_a = jax.random.fold_in(key, 11)
    key_b = jax.random.fold_in(key, 12)
    shape = (3, NX, NY, NZ, RANK)
    position = (jnp.arange(NX, dtype=jnp.float32) + 0.5) / NX
    slab_scale = (0.6 + 1.2 * position).reshape(1, NX, 1, 1, 1)
    rough = jnp.exp(jax.random.uniform(key_b, (3, NX, NY, NZ, 1), jnp.float32, -0.35, 0.35))
    values = jax.random.normal(key_a, shape, jnp.float32)
    values = jnp.clip(values * slab_scale * rough, -8.0, 8.0)
    return values.astype(jnp.bfloat16)


def gaussian(stream_key, extent, width, most, kind=jnp.bfloat16):
    result = width * jax.random.normal(stream_key, extent, jnp.float32)
    return jnp.clip(result, min=-most, max=most).astype(kind)


def setup_inputs(seed: int = 0, part: int = 0) -> dict:
    seeds = jax.random.split(jax.random.key(seed), 5)
    part_splits = jax.random.split(jax.random.fold_in(seeds[4], part), 5)
    return {
        "velocity": draw_velocity(jax.random.fold_in(jax.random.fold_in(seeds[4], part), 71), part),
        "span_rim": draw_span_rim(jax.random.fold_in(jax.random.fold_in(seeds[4], part), 71), part),
        "sketch_old": draw_sketch_old(jax.random.fold_in(jax.random.fold_in(seeds[4], part), 71), part),
        "omega": gaussian(seeds[3], (SNAPS, RANK), 1.0, 6.0, jnp.float32),
    }


COEFS = (0.75, -0.15, 1.0 / 60.0)

def periodic_diff(field, axis):
    total = jnp.zeros(field.shape, jnp.float32)
    for shift_k, weight in zip((1, 2, 3), COEFS):
        total = total + weight * (jnp.roll(field, -shift_k, axis) - jnp.roll(field, shift_k, axis))
    return total

def band_diff(padded, axis, count):
    out_shape = list(padded.shape)
    out_shape[axis] = count
    total = jnp.zeros(tuple(out_shape), jnp.float32)
    for shift_k, weight in zip((1, 2, 3), COEFS):
        ahead = lax.slice_in_dim(padded, 3 + shift_k, 3 + shift_k + count, axis=axis)
        behind = lax.slice_in_dim(padded, 3 - shift_k, 3 - shift_k + count, axis=axis)
        total = total + weight * (ahead - behind)
    return total

def span_extend(field, rim_part):
    return jnp.concatenate([rim_part[..., :3], field, rim_part[..., 3:]], axis=-1)

def upper_factor(gram):
    order = gram.shape[0]
    index = jnp.arange(order, dtype=jnp.int32)

    def column_step(j, lower):
        pick = (index == j).astype(gram.dtype)
        row = jnp.dot(pick, lower, precision=lax.Precision.HIGHEST)
        column = jnp.dot(gram, pick, precision=lax.Precision.HIGHEST) - jnp.dot(lower, row, precision=lax.Precision.HIGHEST)
        pivot = jnp.sqrt(jnp.sum(column * pick))
        below = (index > j).astype(gram.dtype)
        fresh = column * below / pivot + pick * pivot
        return lower + fresh[:, None] * pick[None, :]
    lower = lax.fori_loop(0, order, column_step, jnp.zeros_like(gram))
    return lower.T

def inverse_upper(upper):
    order = upper.shape[0]
    index = jnp.arange(order, dtype=jnp.int32)
    lower = upper.T

    def row_step(j, solved):
        pick = (index == j).astype(upper.dtype)
        row = jnp.dot(pick, lower, precision=lax.Precision.HIGHEST)
        pivot = jnp.sum(row * pick)
        fresh = (pick - jnp.dot(row, solved, precision=lax.Precision.HIGHEST)) / pivot
        return solved + pick[:, None] * fresh[None, :]
    solved = lax.fori_loop(0, order, row_step, jnp.zeros_like(upper))
    return solved.T

def gram_of(matrix):
    return lax.dot_general(matrix, matrix, (((0,), (0,)), ((), ())), preferred_element_type=jnp.float32)

def reference(velocity, span_rim, sketch_old, omega):
    band = velocity[:, :, :, 3:3 + NY]
    u_span = span_extend(band[:, 0], span_rim[:, 0])
    v_span = span_extend(band[:, 1], span_rim[:, 1])
    vort_x = band_diff(velocity[:, 2], 2, NY) - band_diff(v_span, 3, NZ)
    vort_y = band_diff(u_span, 3, NZ) - periodic_diff(band[:, 2], 1)
    vort_z = periodic_diff(band[:, 1], 1) - band_diff(velocity[:, 0], 2, NY)
    vort = jnp.stack([vort_x, vort_y, vort_z], axis=1)
    sketch = sketch_old.astype(jnp.float32)
    for snap in range(SNAPS):
        sketch = sketch + vort[snap][..., None] * omega[snap]
    sketch = sketch.astype(jnp.bfloat16)
    matrix = sketch.reshape(-1, RANK)
    total = jnp.float32(matrix.shape[0])
    factor = upper_factor(gram_of(matrix) / total)
    inverse_one = inverse_upper(factor).astype(jnp.bfloat16)
    basis = jnp.dot(matrix, inverse_one, preferred_element_type=jnp.float32).astype(jnp.bfloat16)
    return (basis.reshape(sketch.shape), factor)
```

```python
import jax
import jax.numpy as jnp
from jax import lax
from jax.sharding import PartitionSpec as P

COEFS = (0.75, -0.15, 1.0 / 60.0)


def extended_2(cells, sides, width):
    for axis, dim in sides:
        count = lax.axis_size(axis)
        head = lax.slice_in_dim(cells, 0, width, axis=dim)
        tail = lax.slice_in_dim(cells, cells.shape[dim] - width, cells.shape[dim], axis=dim)
        cells = jnp.concatenate(
            [
                lax.ppermute(tail, axis, [(i, (i + 1) % count) for i in range(count)]),
                cells,
                lax.ppermute(head, axis, [((i + 1) % count, i) for i in range(count)]),
            ],
            axis=dim,
        )
    return cells


def band_diff(padded, axis, count):
    out_shape = list(padded.shape)
    out_shape[axis] = count
    total = jnp.zeros(tuple(out_shape), jnp.float32)
    for shift_k, weight in zip((1, 2, 3), COEFS):
        ahead = lax.slice_in_dim(padded, 3 + shift_k, 3 + shift_k + count, axis=axis)
        behind = lax.slice_in_dim(padded, 3 - shift_k, 3 - shift_k + count, axis=axis)
        total = total + weight * (ahead - behind)
    return total


def span_extend(field, rim_part):
    return jnp.concatenate([rim_part[..., :3], field, rim_part[..., 3:]], axis=-1)


def upper_factor(gram):
    order = gram.shape[0]
    index = jnp.arange(order, dtype=jnp.int32)

    def column_step(j, lower):
        pick = (index == j).astype(gram.dtype)
        row = jnp.dot(pick, lower, precision=lax.Precision.HIGHEST)
        column = jnp.dot(gram, pick, precision=lax.Precision.HIGHEST) - jnp.dot(
            lower, row, precision=lax.Precision.HIGHEST
        )
        pivot = jnp.sqrt(jnp.sum(column * pick))
        below = (index > j).astype(gram.dtype)
        fresh = column * below / pivot + pick * pivot
        return lower + fresh[:, None] * pick[None, :]

    lower = lax.fori_loop(0, order, column_step, jnp.zeros_like(gram))
    return lower.T


def inverse_upper(upper):
    order = upper.shape[0]
    index = jnp.arange(order, dtype=jnp.int32)
    lower = upper.T

    def row_step(j, solved):
        pick = (index == j).astype(upper.dtype)
        row = jnp.dot(pick, lower, precision=lax.Precision.HIGHEST)
        pivot = jnp.sum(row * pick)
        fresh = (pick - jnp.dot(row, solved, precision=lax.Precision.HIGHEST)) / pivot
        return solved + pick[:, None] * fresh[None, :]

    solved = lax.fori_loop(0, order, row_step, jnp.zeros_like(upper))
    return solved.T


def gram_of(matrix):
    return lax.dot_general(
        matrix, matrix, (((0,), (0,)), ((), ())), preferred_element_type=jnp.float32
    )


def local(velocity, span_rim, sketch_old, omega):
    slabs = velocity.shape[2]
    band_rows = velocity.shape[3] - 6
    span_cells = velocity.shape[4]
    extended = extended_2(velocity, (("gx", 2),), 3)
    v_ext = extended[:, 1, :, 3 : 3 + band_rows]
    w_ext = extended[:, 2, :, 3 : 3 + band_rows]
    band = velocity[:, :, :, 3 : 3 + band_rows]
    u_span = span_extend(band[:, 0], span_rim[:, 0])
    v_span = span_extend(band[:, 1], span_rim[:, 1])
    vort_x = band_diff(velocity[:, 2], 2, band_rows) - band_diff(v_span, 3, span_cells)
    vort_y = band_diff(u_span, 3, span_cells) - band_diff(w_ext, 1, slabs)
    vort_z = band_diff(v_ext, 1, slabs) - band_diff(velocity[:, 0], 2, band_rows)
    vort = jnp.stack([vort_x, vort_y, vort_z], axis=1)
    sketch = sketch_old.astype(jnp.float32)
    for snap in range(vort.shape[0]):
        sketch = sketch + vort[snap][..., None] * omega[snap]
    sketch = sketch.astype(jnp.bfloat16)
    matrix = sketch.reshape(-1, sketch.shape[-1])
    total = jnp.float32(matrix.shape[0] * lax.axis_size("gx"))
    local_gram = gram_of(matrix) / total
    gram = lax.psum(local_gram, "gx")
    lower = lax.linalg.cholesky(gram, symmetrize_input=False)
    factor = lower.T
    eye = jnp.eye(gram.shape[0], dtype=gram.dtype)
    lower_inv = lax.linalg.triangular_solve(lower, eye, left_side=True, lower=True)
    inverse_one = lower_inv.T.astype(jnp.bfloat16)
    basis = jnp.dot(matrix, inverse_one, preferred_element_type=jnp.float32).astype(jnp.bfloat16)
    return (basis.reshape(sketch.shape), factor)


def solution(mesh):
    in_specs = (
        P(None, None, ("rec", "gx"), None, None),
        P(None, None, ("rec", "gx"), None, None),
        P(None, ("rec", "gx"), None, None, None),
        P(),
    )
    out_specs = (P(None, ("rec", "gx"), None, None, None), P("rec", None))
    return jax.shard_map(local, mesh=mesh, in_specs=in_specs, out_specs=out_specs, check_vma=False)
```
